256 devices in a mesh: dp: 32 (over z_lo, y, core), graph: 8 (over z_hi, x).
Axes of the slice: x: 4, y: 4, z: 8 (z_hi: 2, z_lo: 4; z = z_hi * 4 + z_lo), core: 2. Of those that a mesh axis runs over, the one named last changes fastest.
Arguments:
- embedding: bfloat16 [32, 12288, 512], P('dp', 'graph'), may hold values from -6 to 6
- triplet_basis: bfloat16 [32, 49152, 64], P('dp', 'graph'), may hold values from -6 to 6
- atom_cotangent: bfloat16 [32, 768, 1024], P('dp', 'graph'), may hold values from -6 to 6
- fidelity: int32 [32, 768], P('dp', 'graph'), may hold values 0 or 1
- edge_target: int32 [32, 12288], P('dp', 'graph'), may hold values from 0 to 767, as said below
- triplet_source: int32 [32, 49152], P('dp', 'graph'), may hold values from 0 to 12287, as said below
- triplet_target: int32 [32, 49152], P('dp', 'graph'), may hold values from 0 to 12287, as said below
- edge_count: int32 [32, 8], P('dp', 'graph'), may hold values from 768 to 1536, as said below
- triplet_count: int32 [32, 8], P('dp', 'graph'), may hold values from 1536 to 6144, as said below
- w_down: bfloat16 [512, 64], replicated, may hold values from -0.25 to 0.25
- w_up: bfloat16 [64, 512], replicated, may hold values from -0.75 to 0.75
- w_atom: bfloat16 [512, 1024], replicated, may hold values from -0.25 to 0.25
Outputs:
- embedding_grad: bfloat16 [32, 12288, 512], P('dp', 'graph')
- w_atom_grad: float32 [512, 1024], P(None, 'graph')
- w_up_grad: float32 [64, 512], replicated
- w_down_grad: float32 [512, 64], replicated
The draws below stay inside these ranges and needn't reach their ends.
Inputs may be any that keep to these rules, and one draw needn't show every extreme that they name: `edge_target`: edges of index g of graph, slots g * 1536 to (g + 1) * 1536 - 1, have target atoms anywhere in their batch. `triplet_source`: A live edge slot of any index of graph in the same batch. `triplet_target`: A live edge slot of the same index of graph as the triplet slot. `edge_count`: some index of graph of every batch has all 1536 edge slots live. `triplet_count`: some index of graph of every batch has all 6144 triplet slots live.
All inputs are finite; a program needn't handle non-finite values. No bound on the sum of `fidelity` on one device may be relied on, other than what follows from the above.
Results may differ from the reference program's by a relative error of at most 0.0077.
Values may be sent and summed in bfloat16 or wider, within the bound.
No kernel may reach another device: no remote copies, remote signals or barrier semaphores. Data moves between devices by JAX's collectives and lax.ppermute only.
A program may use at most 128 MiB of HBM per device.

```python
import jax
import jax.numpy as jnp
from jax import lax

DA = 1024
DE = 512
DB = 64
ATOM_DEV = 96
EDGE_DEV = 1536
TRIP_DEV = 6144
BATCHES = 32
ATOMS = 768
EDGES = 12288
TRIPS = 49152
N_GRAPH = 8


def linked_edges(key):
    base = jax.random.fold_in(key, 7)
    keys = jax.random.split(base, 6)
    groups = EDGES // EDGE_DEV
    counts = jax.random.randint(keys[0], (BATCHES, groups), EDGE_DEV // 2, EDGE_DEV + 1)
    full = jax.random.randint(keys[1], (BATCHES, 1), 0, groups)
    counts = jnp.where(jnp.arange(groups, dtype=jnp.int32)[None, :] == full, EDGE_DEV, counts).astype(jnp.int32)
    owner = (jnp.arange(TRIPS, dtype=jnp.int32) // TRIP_DEV)[None, :] * jnp.ones((BATCHES, 1), jnp.int32)
    remote = jax.random.randint(keys[2], (BATCHES, TRIPS), 0, groups)
    stay = jax.random.randint(keys[3], (BATCHES, TRIPS), 0, 2)
    holder = jnp.where(stay == 1, owner, remote)
    limit = jnp.take_along_axis(counts, holder, axis=1)
    offset = jax.random.randint(keys[4], (BATCHES, TRIPS), 0, limit)
    source = (holder * EDGE_DEV + offset).astype(jnp.int32)
    own_limit = jnp.take_along_axis(counts, owner, axis=1)
    own_offset = jax.random.randint(keys[5], (BATCHES, TRIPS), 0, own_limit)
    dest = (owner * EDGE_DEV + own_offset).astype(jnp.int32)
    return (counts, source, dest)


def draw_edge_count(key, part):
    return linked_edges(key)[0]


def draw_triplet_source(key, part):
    return linked_edges(key)[1]


def draw_triplet_target(key, part):
    return linked_edges(key)[2]


def draw_triplet_count(key, part):
    base = jax.random.fold_in(key, 11)
    keys = jax.random.split(base, 2)
    groups = TRIPS // TRIP_DEV
    counts = jax.random.randint(keys[0], (BATCHES, groups), TRIP_DEV // 4, TRIP_DEV + 1)
    full = jax.random.randint(keys[1], (BATCHES, 1), 0, groups)
    return jnp.where(jnp.arange(groups, dtype=jnp.int32)[None, :] == full, TRIP_DEV, counts).astype(jnp.int32)


def draw_edge_target(key, part):
    base = jax.random.fold_in(key, 3)
    keys = jax.random.split(base, 3)
    owner = (jnp.arange(EDGES, dtype=jnp.int32) // EDGE_DEV)[None, :]
    near = owner * ATOM_DEV + jax.random.randint(keys[0], (BATCHES, EDGES), 0, ATOM_DEV)
    remote = jax.random.randint(keys[1], (BATCHES, EDGES), 0, ATOMS)
    pick = jax.random.randint(keys[2], (BATCHES, EDGES), 0, 4)
    return jnp.where(pick == 0, remote, near).astype(jnp.int32)


def plant(values, key, smallest, largest):
    longest = values.shape.index(max(values.shape))
    spots = []
    for shift in (0, 1):
        where = [jax.random.randint(jax.random.fold_in(key, axis), (), 0, length) for axis, length in enumerate(values.shape)]
        where[longest] = (where[longest] + shift) % values.shape[longest]
        spots.append(tuple(where))
    return values.at[spots[0]].set(smallest).at[spots[1]].set(largest)


def raised(values, key, source, target, shards_of, factor):
    owner, partner = [(jnp.arange(values.shape[position]) // (values.shape[position] // shards_of)).reshape([-1 if axis == position else 1 for axis in range(values.ndim)]) for position in (source, target)]
    chosen = jax.random.permutation(key, shards_of)[partner]
    strong = (owner == chosen) | (owner == (partner + shards_of // 2) % shards_of)
    return jnp.where(strong, factor * values, values)


def steps_of(rng, extent, cuts, smallest, high):
    def one(axis_at, blocks):
        heights = jax.random.uniform(jax.random.fold_in(jax.random.fold_in(rng, 6), axis_at), (blocks,), jnp.float32, smallest / len(cuts), high / len(cuts))
        return jnp.repeat(jnp.exp(heights), extent[axis_at] // blocks).reshape((-1,) + (1,) * (len(extent) - axis_at - 1))

    level = one(*cuts[0])
    for cut in cuts[1:]:
        level = level * one(*cut)
    return level


def noise(own_key, dims, deviation, most, cuts=(), kind=jnp.bfloat16):
    values = deviation * jax.random.normal(own_key, dims, jnp.float32)
    if cuts:
        values = values * steps_of(own_key, dims, cuts, -0.22, 0.18)
    return jnp.clip(values, -most, most).astype(kind)


def bell_draw_with(stream_key, dims, spread, bound, cuts, heavy, kind=jnp.bfloat16):
    values = spread * jax.random.normal(stream_key, dims, jnp.float32)
    if cuts:
        values = values * steps_of(stream_key, dims, cuts, -0.22, 0.18)
    return jnp.clip(raised(values, jax.random.fold_in(stream_key, 3), *heavy), -bound, bound).astype(kind)


def setup_inputs(seed: int = 0) -> dict:
    streams_of = jax.random.split(jax.random.key(seed), 13)
    return {
        "embedding": noise(streams_of[0], (BATCHES, EDGES, DE), 1.0, 6.0, ((0, 32), (1, 8))),
        "triplet_basis": noise(streams_of[1], (BATCHES, TRIPS, DB), 1.0, 6.0, ((0, 32), (1, 8))),
        "atom_cotangent": bell_draw_with(streams_of[2], (BATCHES, ATOMS, DA), 1.0, 6.0, ((0, 32), (1, 8)), (1, 2, 8, 2.0)),
        "fidelity": plant((jax.random.randint(streams_of[3], (BATCHES, ATOMS), 0, 4) < 1).astype(jnp.int32), jax.random.fold_in(streams_of[3], 1), 0, 1),
        "edge_target": draw_edge_target(jax.random.fold_in(streams_of[12], 71), 0),
        "triplet_source": draw_triplet_source(jax.random.fold_in(streams_of[12], 71), 0),
        "triplet_target": draw_triplet_target(jax.random.fold_in(streams_of[12], 71), 0),
        "edge_count": draw_edge_count(jax.random.fold_in(streams_of[12], 71), 0),
        "triplet_count": draw_triplet_count(jax.random.fold_in(streams_of[12], 71), 0),
        "w_down": noise(streams_of[9], (DE, DB), DE ** -0.5, 0.25),
        "w_up": noise(streams_of[10], (DB, DE), DB ** -0.5, 0.75),
        "w_atom": noise(streams_of[11], (DE, DA), DE ** -0.5, 0.25),
    }


def batch_terms(rows, basis, cotangent, labels, target, source, dest, edge_live_count, trip_live_count, w_down, w_up, w_atom):
    edge_pos = jnp.arange(EDGES, dtype=jnp.int32)
    trip_pos = jnp.arange(TRIPS, dtype=jnp.int32)
    edge_live = (edge_pos % EDGE_DEV) < jnp.take(edge_live_count, edge_pos // EDGE_DEV)
    trip_live = (trip_pos % TRIP_DEV) < jnp.take(trip_live_count, trip_pos // TRIP_DEV)
    weight = 1.0 + 3.0 * labels.astype(jnp.float32)
    scaled = (weight[:, None] * cotangent.astype(jnp.float32)).astype(jnp.bfloat16)
    feats = jnp.dot(jnp.take(rows, source, axis=0), w_down, preferred_element_type=jnp.float32).astype(jnp.bfloat16)
    product = jnp.where(trip_live[:, None], feats.astype(jnp.float32) * basis.astype(jnp.float32), jnp.float32(0.0))
    aggregate = jax.ops.segment_sum(product, dest, num_segments=EDGES).astype(jnp.bfloat16)
    pre = jnp.dot(aggregate, w_up, preferred_element_type=jnp.float32)
    sig = jax.nn.sigmoid(pre)
    updated = (rows.astype(jnp.float32) + pre * sig).astype(jnp.bfloat16)
    edge_in = jnp.where(edge_live[:, None], jnp.take(scaled, target, axis=0), jnp.zeros((), jnp.bfloat16))
    edge_out = jnp.dot(edge_in, w_atom.T, preferred_element_type=jnp.float32)
    part_atom = jnp.dot(updated.T, edge_in, preferred_element_type=jnp.float32)
    pre_grad = (edge_out * sig * (1.0 + pre * (1.0 - sig))).astype(jnp.bfloat16)
    part_up = jnp.dot(aggregate.T, pre_grad, preferred_element_type=jnp.float32)
    aggregate_grad = jnp.dot(pre_grad, w_up.T, preferred_element_type=jnp.float32).astype(jnp.bfloat16)
    contrib = jnp.where(trip_live[:, None], jnp.take(aggregate_grad, dest, axis=0).astype(jnp.float32) * basis.astype(jnp.float32), jnp.float32(0.0))
    total = jnp.zeros((EDGES, DB), jnp.float32)
    for group in range(N_GRAPH):
        piece = contrib[group * TRIP_DEV:(group + 1) * TRIP_DEV]
        piece_source = source[group * TRIP_DEV:(group + 1) * TRIP_DEV]
        partial_grad = jax.ops.segment_sum(piece, piece_source, num_segments=EDGES).astype(jnp.bfloat16)
        partial_grad = lax.optimization_barrier(partial_grad)
        total = total + partial_grad.astype(jnp.float32)
    source_grad = total.astype(jnp.bfloat16)
    part_down = jnp.dot(rows.T, source_grad, preferred_element_type=jnp.float32)
    result = (edge_out + jnp.dot(source_grad, w_down.T, preferred_element_type=jnp.float32)).astype(jnp.bfloat16)
    return result, part_atom, part_up, part_down


def reference(embedding, triplet_basis, atom_cotangent, fidelity, edge_target, triplet_source, triplet_target, edge_count, triplet_count, w_down, w_up, w_atom):
    def step_batch(carry, items):
        result, part_atom, part_up, part_down = batch_terms(*items, w_down, w_up, w_atom)
        return (carry[0] + part_atom, carry[1] + part_up, carry[2] + part_down), result

    start = (jnp.zeros((DE, DA), jnp.float32), jnp.zeros((DB, DE), jnp.float32), jnp.zeros((DE, DB), jnp.float32))
    sums, results = lax.scan(step_batch, start, (embedding, triplet_basis, atom_cotangent, fidelity, edge_target, triplet_source, triplet_target, edge_count, triplet_count))
    return (results, sums[0], sums[1], sums[2])
```

```python
import jax
import jax.numpy as jnp
from jax import lax
from jax.sharding import PartitionSpec as P


def shifted(x, axis, size, k):
    return lax.ppermute(x, axis, [(i, (i + k) % size) for i in range(size)])


def butterfly(x, axis, size):
    bit = 1
    while bit < size:
        x = x + lax.ppermute(x, axis, [(i, i ^ bit) for i in range(size)])
        bit *= 2
    return x


def local(
    embedding,
    triplet_basis,
    atom_cotangent,
    fidelity,
    edge_target,
    triplet_source,
    triplet_target,
    edge_count,
    triplet_count,
    w_down,
    w_up,
    w_atom,
):
    rows = embedding[0]
    basis = triplet_basis[0]
    edge_slots, de = rows.shape
    trip_slots, db = basis.shape
    atom_slots, da = atom_cotangent.shape[1:]
    groups = lax.axis_size("graph")
    dps = lax.axis_size("dp")
    here = lax.axis_index("graph")
    edge_live = jnp.arange(edge_slots, dtype=jnp.int32) < edge_count[0, 0]
    trip_live = jnp.arange(trip_slots, dtype=jnp.int32) < triplet_count[0, 0]
    weight = 1.0 + 3.0 * fidelity[0].astype(jnp.float32)
    scaled = (weight[:, None] * atom_cotangent[0].astype(jnp.float32)).astype(jnp.bfloat16)
    projected = jnp.dot(rows, w_down, preferred_element_type=jnp.float32).astype(jnp.bfloat16)

    packed = jnp.concatenate([scaled.reshape(-1), projected.reshape(-1)])
    pieces = [packed] + [shifted(packed, "graph", groups, k) for k in range(1, groups)]
    got = jnp.stack(pieces)
    n_atom = atom_slots * da
    atoms_all = got[:, :n_atom].reshape(groups * atom_slots, da)
    table = got[:, n_atom:].reshape(groups * edge_slots, db)

    source = triplet_source[0]
    src_row = ((here - source // edge_slots) % groups) * edge_slots + source % edge_slots
    feats = jnp.take(table, src_row, axis=0)
    target = edge_target[0]
    tgt_row = ((here - target // atom_slots) % groups) * atom_slots + target % atom_slots

    local_dest = triplet_target[0] - here * edge_slots
    product = feats.astype(jnp.float32) * basis.astype(jnp.float32)
    hi = product.astype(jnp.bfloat16)
    lo = (product - hi.astype(jnp.float32)).astype(jnp.bfloat16)
    pick = (local_dest[None, :] == jnp.arange(edge_slots, dtype=jnp.int32)[:, None]) & trip_live[None, :]
    summed = jnp.dot(
        pick.astype(jnp.bfloat16),
        jnp.concatenate([hi, lo], axis=1),
        preferred_element_type=jnp.float32,
    )
    aggregate = (summed[:, :db] + summed[:, db:]).astype(jnp.bfloat16)

    pre = jnp.dot(aggregate, w_up, preferred_element_type=jnp.float32)
    sig = jax.nn.sigmoid(pre)
    updated = (rows.astype(jnp.float32) + pre * sig).astype(jnp.bfloat16)
    edge_in = jnp.where(
        edge_live[:, None], jnp.take(atoms_all, tgt_row, axis=0), jnp.zeros((), jnp.bfloat16)
    )
    edge_out = jnp.dot(edge_in, w_atom.T, preferred_element_type=jnp.float32)
    part_atom = jnp.dot(updated.T, edge_in, preferred_element_type=jnp.float32)
    pre_grad = (edge_out * sig * (1.0 + pre * (1.0 - sig))).astype(jnp.bfloat16)
    part_up = jnp.dot(aggregate.T, pre_grad, preferred_element_type=jnp.float32)
    aggregate_grad = jnp.dot(pre_grad, w_up.T, preferred_element_type=jnp.float32).astype(
        jnp.bfloat16
    )
    contrib = jnp.where(
        trip_live[:, None],
        jnp.take(aggregate_grad, local_dest, axis=0).astype(jnp.float32)
        * basis.astype(jnp.float32),
        jnp.float32(0.0),
    )
    partial_grad = jax.ops.segment_sum(
        contrib, source, num_segments=edge_slots * groups
    ).astype(jnp.bfloat16)
    blocks = partial_grad.reshape(groups, edge_slots, db)
    total = jnp.take(blocks, here, axis=0).astype(jnp.float32)
    for k in range(1, groups):
        piece = jnp.take(blocks, (here + k) % groups, axis=0)
        total = total + shifted(piece, "graph", groups, k).astype(jnp.float32)
    source_grad = total.astype(jnp.bfloat16)
    part_down = jnp.dot(rows.T, source_grad, preferred_element_type=jnp.float32)
    result = (edge_out + jnp.dot(source_grad, w_down.T, preferred_element_type=jnp.float32)).astype(
        jnp.bfloat16
    )

    width = da // groups
    atom_blocks = part_atom.reshape(de, groups, width)
    atom_sum = jnp.take(atom_blocks, here, axis=1)
    for k in range(1, groups):
        piece = jnp.take(atom_blocks, (here + k) % groups, axis=1)
        atom_sum = atom_sum + shifted(piece, "graph", groups, k)
    small = butterfly(jnp.concatenate([part_up.T, part_down], axis=1), "graph", groups)
    both = butterfly(jnp.concatenate([atom_sum, small], axis=1), "dp", dps)
    atom_grad = both[:, :width]
    up_grad = both[:, width : width + db].T
    down_grad = both[:, width + db :]
    return (result[None], atom_grad, up_grad, down_grad)


def solution(mesh):
    return jax.shard_map(
        local,
        mesh=mesh,
        in_specs=(
            P("dp", "graph", None),
            P("dp", "graph", None),
            P("dp", "graph", None),
            P("dp", "graph"),
            P("dp", "graph"),
            P("dp", "graph"),
            P("dp", "graph"),
            P("dp", "graph"),
            P("dp", "graph"),
            P(),
            P(),
            P(),
        ),
        out_specs=(P("dp", "graph", None), P(None, "graph"), P(), P()),
        check_vma=False,
    )
```

```python
import jax
import jax.numpy as jnp
from jax import lax
from jax.sharding import PartitionSpec as P


def shifted(x, axis, size, k):
    return lax.ppermute(x, axis, [(i, (i + k) % size) for i in range(size)])


def butterfly(x, axis, size):
    bit = 1
    while bit < size:
        x = x + lax.ppermute(x, axis, [(i, i ^ bit) for i in range(size)])
        bit *= 2
    return x


def local(
    embedding,
    triplet_basis,
    atom_cotangent,
    fidelity,
    edge_target,
    triplet_source,
    triplet_target,
    edge_count,
    triplet_count,
    w_down,
    w_up,
    w_atom,
):
    rows = embedding[0]
    basis = triplet_basis[0]
    edge_slots, de = rows.shape
    trip_slots, db = basis.shape
    atom_slots, da = atom_cotangent.shape[1:]
    groups = lax.axis_size("graph")
    dps = lax.axis_size("dp")
    here = lax.axis_index("graph")
    edge_live = jnp.arange(edge_slots, dtype=jnp.int32) < edge_count[0, 0]
    trip_live = jnp.arange(trip_slots, dtype=jnp.int32) < triplet_count[0, 0]
    weight = 1.0 + 3.0 * fidelity[0].astype(jnp.float32)
    scaled = (weight[:, None] * atom_cotangent[0].astype(jnp.float32)).astype(jnp.bfloat16)
    projected = jnp.dot(rows, w_down, preferred_element_type=jnp.float32).astype(jnp.bfloat16)

    atom_pieces = [scaled] + [shifted(scaled, "graph", groups, k) for k in range(1, groups)]
    table_pieces = [projected] + [shifted(projected, "graph", groups, k) for k in range(1, groups)]
    atoms_all = jnp.concatenate(atom_pieces, axis=0)
    table = jnp.concatenate(table_pieces, axis=0)

    source = triplet_source[0]
    src_row = ((here - source // edge_slots) % groups) * edge_slots + source % edge_slots
    feats = jnp.take(table, src_row, axis=0)
    target = edge_target[0]
    tgt_row = ((here - target // atom_slots) % groups) * atom_slots + target % atom_slots

    local_dest = triplet_target[0] - here * edge_slots
    product = feats.astype(jnp.float32) * basis.astype(jnp.float32)
    hi = product.astype(jnp.bfloat16)
    lo = (product - hi.astype(jnp.float32)).astype(jnp.bfloat16)
    pick = (local_dest[None, :] == jnp.arange(edge_slots, dtype=jnp.int32)[:, None]) & trip_live[None, :]
    summed = jnp.dot(
        pick.astype(jnp.bfloat16),
        jnp.concatenate([hi, lo], axis=1),
        preferred_element_type=jnp.float32,
    )
    aggregate = (summed[:, :db] + summed[:, db:]).astype(jnp.bfloat16)

    pre = jnp.dot(aggregate, w_up, preferred_element_type=jnp.float32)
    sig = jax.nn.sigmoid(pre)
    updated = (rows.astype(jnp.float32) + pre * sig).astype(jnp.bfloat16)
    edge_in = jnp.where(
        edge_live[:, None], jnp.take(atoms_all, tgt_row, axis=0), jnp.zeros((), jnp.bfloat16)
    )
    edge_out = jnp.dot(edge_in, w_atom.T, preferred_element_type=jnp.float32)
    part_atom = jnp.dot(updated.T, edge_in, preferred_element_type=jnp.float32)
    pre_grad = (edge_out * sig * (1.0 + pre * (1.0 - sig))).astype(jnp.bfloat16)
    part_up = jnp.dot(aggregate.T, pre_grad, preferred_element_type=jnp.float32)
    aggregate_grad = jnp.dot(pre_grad, w_up.T, preferred_element_type=jnp.float32).astype(
        jnp.bfloat16
    )
    contrib = jnp.where(
        trip_live[:, None],
        jnp.take(aggregate_grad, local_dest, axis=0).astype(jnp.float32)
        * basis.astype(jnp.float32),
        jnp.float32(0.0),
    )
    partial_grad = jax.ops.segment_sum(
        contrib, source, num_segments=edge_slots * groups
    ).astype(jnp.bfloat16)
    blocks = partial_grad.reshape(groups, edge_slots, db)
    total = jnp.take(blocks, here, axis=0).astype(jnp.float32)
    for k in range(1, groups):
        piece = jnp.take(blocks, (here + k) % groups, axis=0)
        total = total + shifted(piece, "graph", groups, k).astype(jnp.float32)
    source_grad = total.astype(jnp.bfloat16)
    part_down = jnp.dot(rows.T, source_grad, preferred_element_type=jnp.float32)
    result = (edge_out + jnp.dot(source_grad, w_down.T, preferred_element_type=jnp.float32)).astype(
        jnp.bfloat16
    )

    width = da // groups
    atom_blocks = part_atom.reshape(de, groups, width)
    atom_sum = jnp.take(atom_blocks, here, axis=1)
    for k in range(1, groups):
        piece = jnp.take(atom_blocks, (here + k) % groups, axis=1)
        atom_sum = atom_sum + shifted(piece, "graph", groups, k)
    up_sum = butterfly(part_up.T, "graph", groups)
    early = butterfly(jnp.concatenate([atom_sum, up_sum], axis=1), "dp", dps)
    down_grad = butterfly(butterfly(part_down, "graph", groups), "dp", dps)
    atom_grad = early[:, :width]
    up_grad = early[:, width:].T
    return (result[None], atom_grad, up_grad, down_grad)


def solution(mesh):
    return jax.shard_map(
        local,
        mesh=mesh,
        in_specs=(
            P("dp", "graph", None),
            P("dp", "graph", None),
            P("dp", "graph", None),
            P("dp", "graph"),
            P("dp", "graph"),
            P("dp", "graph"),
            P("dp", "graph"),
            P("dp", "graph"),
            P("dp", "graph"),
            P(),
            P(),
            P(),
        ),
        out_specs=(P("dp", "graph", None), P(None, "graph"), P(), P()),
        check_vma=False,
    )
```

```python
import jax
import jax.numpy as jnp
from jax import lax
from jax.sharding import PartitionSpec as P


def shifted(x, axis, size, k):
    return lax.ppermute(x, axis, [(i, (i + k) % size) for i in range(size)])


def butterfly(x, axis, size):
    bit = 1
    while bit < size:
        x = x + lax.ppermute(x, axis, [(i, i ^ bit) for i in range(size)])
        bit *= 2
    return x


def local(
    embedding,
    triplet_basis,
    atom_cotangent,
    fidelity,
    edge_target,
    triplet_source,
    triplet_target,
    edge_count,
    triplet_count,
    w_down,
    w_up,
    w_atom,
):
    rows = embedding[0]
    basis = triplet_basis[0]
    edge_slots, de = rows.shape
    trip_slots, db = basis.shape
    atom_slots, da = atom_cotangent.shape[1:]
    groups = lax.axis_size("graph")
    dps = lax.axis_size("dp")
    here = lax.axis_index("graph")
    edge_live = jnp.arange(edge_slots, dtype=jnp.int32) < edge_count[0, 0]
    trip_live = jnp.arange(trip_slots, dtype=jnp.int32) < triplet_count[0, 0]
    weight = 1.0 + 3.0 * fidelity[0].astype(jnp.float32)
    scaled = (weight[:, None] * atom_cotangent[0].astype(jnp.float32)).astype(jnp.bfloat16)
    projected = jnp.dot(rows, w_down, preferred_element_type=jnp.float32).astype(jnp.bfloat16)

    packed = jnp.concatenate([scaled, projected.reshape(-1, da)], axis=0)
    pieces = [packed] + [shifted(packed, "graph", groups, k) for k in range(1, groups)]
    atoms_all = jnp.concatenate([p[:atom_slots] for p in pieces], axis=0)
    table = jnp.concatenate([p[atom_slots:].reshape(-1, 2 * db) for p in pieces], axis=0)

    source = triplet_source[0]
    src_row = ((here - source // edge_slots) % groups) * edge_slots + source % edge_slots
    pair = jnp.take(table, src_row // 2, axis=0)
    feats = jnp.where((src_row % 2 == 0)[:, None], pair[:, :db], pair[:, db:])
    target = edge_target[0]
    tgt_row = ((here - target // atom_slots) % groups) * atom_slots + target % atom_slots

    local_dest = triplet_target[0] - here * edge_slots
    product = feats.astype(jnp.float32) * basis.astype(jnp.float32)
    hi = product.astype(jnp.bfloat16)
    lo = (product - hi.astype(jnp.float32)).astype(jnp.bfloat16)
    pick = (local_dest[None, :] == jnp.arange(edge_slots, dtype=jnp.int32)[:, None]) & trip_live[None, :]
    summed = jnp.dot(
        pick.astype(jnp.bfloat16),
        jnp.concatenate([hi, lo], axis=1),
        preferred_element_type=jnp.float32,
    )
    aggregate = (summed[:, :db] + summed[:, db:]).astype(jnp.bfloat16)

    pre = jnp.dot(aggregate, w_up, preferred_element_type=jnp.float32)
    sig = jax.nn.sigmoid(pre)
    updated = (rows.astype(jnp.float32) + pre * sig).astype(jnp.bfloat16)
    edge_in = jnp.where(
        edge_live[:, None], jnp.take(atoms_all, tgt_row, axis=0), jnp.zeros((), jnp.bfloat16)
    )
    edge_out = jnp.dot(edge_in, w_atom.T, preferred_element_type=jnp.float32)
    part_atom = jnp.dot(updated.T, edge_in, preferred_element_type=jnp.float32)
    pre_grad = (edge_out * sig * (1.0 + pre * (1.0 - sig))).astype(jnp.bfloat16)
    part_up = jnp.dot(aggregate.T, pre_grad, preferred_element_type=jnp.float32)
    aggregate_grad = jnp.dot(pre_grad, w_up.T, preferred_element_type=jnp.float32).astype(
        jnp.bfloat16
    )
    contrib = jnp.where(
        trip_live[:, None],
        jnp.take(aggregate_grad, local_dest, axis=0).astype(jnp.float32)
        * basis.astype(jnp.float32),
        jnp.float32(0.0),
    )
    partial_grad = jax.ops.segment_sum(
        contrib, source, num_segments=edge_slots * groups
    ).astype(jnp.bfloat16)
    blocks = partial_grad.reshape(groups, edge_slots, db)
    total = jnp.take(blocks, here, axis=0).astype(jnp.float32)
    for k in range(1, groups):
        piece = jnp.take(blocks, (here + k) % groups, axis=0)
        total = total + shifted(piece, "graph", groups, k).astype(jnp.float32)
    source_grad = total.astype(jnp.bfloat16)
    part_down = jnp.dot(rows.T, source_grad, preferred_element_type=jnp.float32)
    result = (edge_out + jnp.dot(source_grad, w_down.T, preferred_element_type=jnp.float32)).astype(
        jnp.bfloat16
    )

    width = da // groups
    atom_blocks = part_atom.reshape(de, groups, width)
    atom_sum = jnp.take(atom_blocks, here, axis=1)
    for k in range(1, groups):
        piece = jnp.take(atom_blocks, (here + k) % groups, axis=1)
        atom_sum = atom_sum + shifted(piece, "graph", groups, k)
    up_sum = butterfly(part_up.T, "graph", groups)
    early = butterfly(jnp.concatenate([atom_sum, up_sum], axis=1), "dp", dps)
    down_grad = butterfly(butterfly(part_down, "graph", groups), "dp", dps)
    atom_grad = early[:, :width]
    up_grad = early[:, width:].T
    return (result[None], atom_grad, up_grad, down_grad)


def solution(mesh):
    return jax.shard_map(
        local,
        mesh=mesh,
        in_specs=(
            P("dp", "graph", None),
            P("dp", "graph", None),
            P("dp", "graph", None),
            P("dp", "graph"),
            P("dp", "graph"),
            P("dp", "graph"),
            P("dp", "graph"),
            P("dp", "graph"),
            P("dp", "graph"),
            P(),
            P(),
            P(),
        ),
        out_specs=(P("dp", "graph", None), P(None, "graph"), P(), P()),
        check_vma=False,
    )
```

```python
import jax
import jax.numpy as jnp
from jax import lax
from jax.sharding import PartitionSpec as P


def shifted(x, axis, size, k):
    return lax.ppermute(x, axis, [(i, (i + k) % size) for i in range(size)])


def butterfly(x, axis, size):
    idx = lax.axis_index(axis)
    stride = 1
    while stride < size:
        radix = 4 if (size // stride) % 4 == 0 else 2
        if radix == 2:
            x = x + lax.ppermute(x, axis, [(i, i ^ stride) for i in range(size)])
        else:
            digit = (idx // stride) % radix
            got = [x]
            for s in range(1, radix):
                pairs = []
                for i in range(size):
                    d = (i // stride) % radix
                    pairs.append((i, i + ((d + s) % radix - d) * stride))
                got.append(lax.ppermute(x, axis, pairs))
            stacked = jnp.stack(got)
            member = [jnp.take(stacked, (digit - m) % radix, axis=0) for m in range(radix)]
            x = (member[0] + member[1]) + (member[2] + member[3])
        stride *= radix
    return x


def local(
    embedding,
    triplet_basis,
    atom_cotangent,
    fidelity,
    edge_target,
    triplet_source,
    triplet_target,
    edge_count,
    triplet_count,
    w_down,
    w_up,
    w_atom,
):
    rows = embedding[0]
    basis = triplet_basis[0]
    edge_slots, de = rows.shape
    trip_slots, db = basis.shape
    atom_slots, da = atom_cotangent.shape[1:]
    groups = lax.axis_size("graph")
    dps = lax.axis_size("dp")
    here = lax.axis_index("graph")
    edge_live = jnp.arange(edge_slots, dtype=jnp.int32) < edge_count[0, 0]
    trip_live = jnp.arange(trip_slots, dtype=jnp.int32) < triplet_count[0, 0]
    weight = 1.0 + 3.0 * fidelity[0].astype(jnp.float32)
    scaled = (weight[:, None] * atom_cotangent[0].astype(jnp.float32)).astype(jnp.bfloat16)
    projected = jnp.dot(rows, w_down, preferred_element_type=jnp.float32).astype(jnp.bfloat16)

    atom_pieces = [scaled] + [shifted(scaled, "graph", groups, k) for k in range(1, groups)]
    table_pieces = [projected] + [shifted(projected, "graph", groups, k) for k in range(1, groups)]
    atoms_all = jnp.concatenate(atom_pieces, axis=0)
    table = jnp.concatenate(table_pieces, axis=0)

    source = triplet_source[0]
    src_row = ((here - source // edge_slots) % groups) * edge_slots + source % edge_slots
    feats = jnp.take(table, src_row, axis=0)
    target = edge_target[0]
    tgt_row = ((here - target // atom_slots) % groups) * atom_slots + target % atom_slots

    local_dest = triplet_target[0] - here * edge_slots
    product = feats.astype(jnp.float32) * basis.astype(jnp.float32)
    hi = product.astype(jnp.bfloat16)
    lo = (product - hi.astype(jnp.float32)).astype(jnp.bfloat16)
    pick = (local_dest[None, :] == jnp.arange(edge_slots, dtype=jnp.int32)[:, None]) & trip_live[None, :]
    summed = jnp.dot(
        pick.astype(jnp.bfloat16),
        jnp.concatenate([hi, lo], axis=1),
        preferred_element_type=jnp.float32,
    )
    aggregate = (summed[:, :db] + summed[:, db:]).astype(jnp.bfloat16)

    pre = jnp.dot(aggregate, w_up, preferred_element_type=jnp.float32)
    sig = jax.nn.sigmoid(pre)
    updated = (rows.astype(jnp.float32) + pre * sig).astype(jnp.bfloat16)
    edge_in = jnp.where(
        edge_live[:, None], jnp.take(atoms_all, tgt_row, axis=0), jnp.zeros((), jnp.bfloat16)
    )
    edge_out = jnp.dot(edge_in, w_atom.T, preferred_element_type=jnp.float32)
    part_atom = jnp.dot(updated.T, edge_in, preferred_element_type=jnp.float32)
    pre_grad = (edge_out * sig * (1.0 + pre * (1.0 - sig))).astype(jnp.bfloat16)
    part_up = jnp.dot(aggregate.T, pre_grad, preferred_element_type=jnp.float32)
    aggregate_grad = jnp.dot(pre_grad, w_up.T, preferred_element_type=jnp.float32).astype(
        jnp.bfloat16
    )
    contrib = jnp.where(
        trip_live[:, None],
        jnp.take(aggregate_grad, local_dest, axis=0).astype(jnp.float32)
        * basis.astype(jnp.float32),
        jnp.float32(0.0),
    )
    partial_grad = jax.ops.segment_sum(
        contrib, source, num_segments=edge_slots * groups
    ).astype(jnp.bfloat16)
    blocks = partial_grad.reshape(groups, edge_slots, db)
    total = jnp.take(blocks, here, axis=0).astype(jnp.float32)
    for k in range(1, groups):
        piece = jnp.take(blocks, (here + k) % groups, axis=0)
        total = total + shifted(piece, "graph", groups, k).astype(jnp.float32)
    source_grad = total.astype(jnp.bfloat16)
    part_down = jnp.dot(rows.T, source_grad, preferred_element_type=jnp.float32)
    result = (edge_out + jnp.dot(source_grad, w_down.T, preferred_element_type=jnp.float32)).astype(
        jnp.bfloat16
    )

    width = da // groups
    atom_blocks = part_atom.reshape(de, groups, width)
    atom_sum = jnp.take(atom_blocks, here, axis=1)
    for k in range(1, groups):
        piece = jnp.take(atom_blocks, (here + k) % groups, axis=1)
        atom_sum = atom_sum + shifted(piece, "graph", groups, k)
    up_sum = butterfly(part_up.T, "graph", groups)
    early = butterfly(jnp.concatenate([atom_sum, up_sum], axis=1), "dp", dps)
    down_grad = butterfly(butterfly(part_down, "graph", groups), "dp", dps)
    atom_grad = early[:, :width]
    up_grad = early[:, width:].T
    return (result[None], atom_grad, up_grad, down_grad)


def solution(mesh):
    return jax.shard_map(
        local,
        mesh=mesh,
        in_specs=(
            P("dp", "graph", None),
            P("dp", "graph", None),
            P("dp", "graph", None),
            P("dp", "graph"),
            P("dp", "graph"),
            P("dp", "graph"),
            P("dp", "graph"),
            P("dp", "graph"),
            P("dp", "graph"),
            P(),
            P(),
            P(),
        ),
        out_specs=(P("dp", "graph", None), P(None, "graph"), P(), P()),
        check_vma=False,
    )
```

```python
import jax
import jax.numpy as jnp
from jax import lax
from jax.sharding import PartitionSpec as P


def shifted(x, axis, size, k):
    return lax.ppermute(x, axis, [(i, (i + k) % size) for i in range(size)])


def butterfly(x, axis, size):
    idx = lax.axis_index(axis)
    stride = 1
    while stride < size:
        radix = 4 if (size // stride) % 4 == 0 else 2
        if radix == 2:
            x = x + lax.ppermute(x, axis, [(i, i ^ stride) for i in range(size)])
        else:
            digit = (idx // stride) % radix
            got = [x]
            for s in range(1, radix):
                pairs = []
                for i in range(size):
                    d = (i // stride) % radix
                    pairs.append((i, i + ((d + s) % radix - d) * stride))
                got.append(lax.ppermute(x, axis, pairs))
            stacked = jnp.stack(got)
            member = [jnp.take(stacked, (digit - m) % radix, axis=0) for m in range(radix)]
            x = (member[0] + member[1]) + (member[2] + member[3])
        stride *= radix
    return x


def local(
    embedding,
    triplet_basis,
    atom_cotangent,
    fidelity,
    edge_target,
    triplet_source,
    triplet_target,
    edge_count,
    triplet_count,
    w_down,
    w_up,
    w_atom,
):
    rows = embedding[0]
    basis = triplet_basis[0]
    edge_slots, de = rows.shape
    trip_slots, db = basis.shape
    atom_slots, da = atom_cotangent.shape[1:]
    groups = lax.axis_size("graph")
    dps = lax.axis_size("dp")
    here = lax.axis_index("graph")
    edge_live = jnp.arange(edge_slots, dtype=jnp.int32) < edge_count[0, 0]
    trip_live = jnp.arange(trip_slots, dtype=jnp.int32) < triplet_count[0, 0]
    weight = 1.0 + 3.0 * fidelity[0].astype(jnp.float32)
    scaled = (weight[:, None] * atom_cotangent[0].astype(jnp.float32)).astype(jnp.bfloat16)
    projected = jnp.dot(rows, w_down, preferred_element_type=jnp.float32).astype(jnp.bfloat16)

    table_pieces = [projected] + [shifted(projected, "graph", groups, k) for k in range(1, groups)]
    atoms_all = lax.all_gather(scaled, "graph", axis=0, tiled=True)
    table = jnp.concatenate(table_pieces, axis=0)

    source = triplet_source[0]
    src_row = ((here - source // edge_slots) % groups) * edge_slots + source % edge_slots
    feats = jnp.take(table, src_row, axis=0)
    target = edge_target[0]

    local_dest = triplet_target[0] - here * edge_slots
    product = feats.astype(jnp.float32) * basis.astype(jnp.float32)
    hi = product.astype(jnp.bfloat16)
    lo = (product - hi.astype(jnp.float32)).astype(jnp.bfloat16)
    pick = (local_dest[None, :] == jnp.arange(edge_slots, dtype=jnp.int32)[:, None]) & trip_live[None, :]
    summed = jnp.dot(
        pick.astype(jnp.bfloat16),
        jnp.concatenate([hi, lo], axis=1),
        preferred_element_type=jnp.float32,
    )
    aggregate = (summed[:, :db] + summed[:, db:]).astype(jnp.bfloat16)

    pre = jnp.dot(aggregate, w_up, preferred_element_type=jnp.float32)
    sig = jax.nn.sigmoid(pre)
    updated = (rows.astype(jnp.float32) + pre * sig).astype(jnp.bfloat16)
    edge_in = jnp.where(
        edge_live[:, None], jnp.take(atoms_all, target, axis=0), jnp.zeros((), jnp.bfloat16)
    )
    edge_out = jnp.dot(edge_in, w_atom.T, preferred_element_type=jnp.float32)
    part_atom = jnp.dot(updated.T, edge_in, preferred_element_type=jnp.float32)
    pre_grad = (edge_out * sig * (1.0 + pre * (1.0 - sig))).astype(jnp.bfloat16)
    part_up = jnp.dot(aggregate.T, pre_grad, preferred_element_type=jnp.float32)
    aggregate_grad = jnp.dot(pre_grad, w_up.T, preferred_element_type=jnp.float32).astype(
        jnp.bfloat16
    )
    contrib = jnp.where(
        trip_live[:, None],
        jnp.take(aggregate_grad, local_dest, axis=0).astype(jnp.float32)
        * basis.astype(jnp.float32),
        jnp.float32(0.0),
    )
    partial_grad = jax.ops.segment_sum(
        contrib, source, num_segments=edge_slots * groups
    ).astype(jnp.bfloat16)
    blocks = partial_grad.reshape(groups, edge_slots, db)
    total = jnp.take(blocks, here, axis=0).astype(jnp.float32)
    for k in range(1, groups):
        piece = jnp.take(blocks, (here + k) % groups, axis=0)
        total = total + shifted(piece, "graph", groups, k).astype(jnp.float32)
    source_grad = total.astype(jnp.bfloat16)
    part_down = jnp.dot(rows.T, source_grad, preferred_element_type=jnp.float32)
    result = (edge_out + jnp.dot(source_grad, w_down.T, preferred_element_type=jnp.float32)).astype(
        jnp.bfloat16
    )

    width = da // groups
    atom_blocks = part_atom.reshape(de, groups, width)
    atom_sum = jnp.take(atom_blocks, here, axis=1)
    for k in range(1, groups):
        piece = jnp.take(atom_blocks, (here + k) % groups, axis=1)
        atom_sum = atom_sum + shifted(piece, "graph", groups, k)
    up_sum = butterfly(part_up.T, "graph", groups)
    early = butterfly(jnp.concatenate([atom_sum, up_sum], axis=1), "dp", dps)
    down_grad = butterfly(butterfly(part_down, "graph", groups), "dp", dps)
    atom_grad = early[:, :width]
    up_grad = early[:, width:].T
    return (result[None], atom_grad, up_grad, down_grad)


def solution(mesh):
    return jax.shard_map(
        local,
        mesh=mesh,
        in_specs=(
            P("dp", "graph", None),
            P("dp", "graph", None),
            P("dp", "graph", None),
            P("dp", "graph"),
            P("dp", "graph"),
            P("dp", "graph"),
            P("dp", "graph"),
            P("dp", "graph"),
            P("dp", "graph"),
            P(),
            P(),
            P(),
        ),
        out_specs=(P("dp", "graph", None), P(None, "graph"), P(), P()),
        check_vma=False,
    )
```

```python
import jax
import jax.numpy as jnp
from jax import lax
from jax.sharding import PartitionSpec as P


def shifted(x, axis, size, k):
    return lax.ppermute(x, axis, [(i, (i + k) % size) for i in range(size)])


def butterfly(x, axis, size):
    idx = lax.axis_index(axis)
    stride = 1
    while stride < size:
        radix = 4 if (size // stride) % 4 == 0 else 2
        if radix == 2:
            x = x + lax.ppermute(x, axis, [(i, i ^ stride) for i in range(size)])
        else:
            digit = (idx // stride) % radix
            got = [x]
            for s in range(1, radix):
                pairs = []
                for i in range(size):
                    d = (i // stride) % radix
                    pairs.append((i, i + ((d + s) % radix - d) * stride))
                got.append(lax.ppermute(x, axis, pairs))
            stacked = jnp.stack(got)
            member = [jnp.take(stacked, (digit - m) % radix, axis=0) for m in range(radix)]
            x = (member[0] + member[1]) + (member[2] + member[3])
        stride *= radix
    return x


def local(
    embedding,
    triplet_basis,
    atom_cotangent,
    fidelity,
    edge_target,
    triplet_source,
    triplet_target,
    edge_count,
    triplet_count,
    w_down,
    w_up,
    w_atom,
):
    rows = embedding[0]
    basis = triplet_basis[0]
    edge_slots, de = rows.shape
    trip_slots, db = basis.shape
    atom_slots, da = atom_cotangent.shape[1:]
    groups = lax.axis_size("graph")
    dps = lax.axis_size("dp")
    here = lax.axis_index("graph")
    edge_live = jnp.arange(edge_slots, dtype=jnp.int32) < edge_count[0, 0]
    trip_live = jnp.arange(trip_slots, dtype=jnp.int32) < triplet_count[0, 0]
    weight = 1.0 + 3.0 * fidelity[0].astype(jnp.float32)
    scaled = (weight[:, None] * atom_cotangent[0].astype(jnp.float32)).astype(jnp.bfloat16)
    projected = jnp.dot(rows, w_down, preferred_element_type=jnp.float32).astype(jnp.bfloat16)

    table_pieces = [projected] + [shifted(projected, "graph", groups, k) for k in range(1, groups)]
    atoms_all = lax.all_gather(scaled, "graph", axis=0, tiled=True)
    table = jnp.concatenate(table_pieces, axis=0)

    source = triplet_source[0]
    src_row = ((here - source // edge_slots) % groups) * edge_slots + source % edge_slots
    feats = jnp.take(table, src_row, axis=0)
    target = edge_target[0]

    local_dest = triplet_target[0] - here * edge_slots
    product = feats.astype(jnp.float32) * basis.astype(jnp.float32)
    hi = product.astype(jnp.bfloat16)
    lo = (product - hi.astype(jnp.float32)).astype(jnp.bfloat16)
    pick = (local_dest[None, :] == jnp.arange(edge_slots, dtype=jnp.int32)[:, None]) & trip_live[None, :]
    summed = jnp.dot(
        pick.astype(jnp.bfloat16),
        jnp.concatenate([hi, lo], axis=1),
        preferred_element_type=jnp.float32,
    )
    aggregate = (summed[:, :db] + summed[:, db:]).astype(jnp.bfloat16)

    pre = jnp.dot(aggregate, w_up, preferred_element_type=jnp.float32)
    sig = jax.nn.sigmoid(pre)
    updated = (rows.astype(jnp.float32) + pre * sig).astype(jnp.bfloat16)
    edge_in = jnp.where(
        edge_live[:, None], jnp.take(atoms_all, target, axis=0), jnp.zeros((), jnp.bfloat16)
    )
    edge_out = jnp.dot(edge_in, w_atom.T, preferred_element_type=jnp.float32)
    part_atom = jnp.dot(updated.T, edge_in, preferred_element_type=jnp.float32)
    pre_grad = (edge_out * sig * (1.0 + pre * (1.0 - sig))).astype(jnp.bfloat16)
    part_up = jnp.dot(aggregate.T, pre_grad, preferred_element_type=jnp.float32)
    aggregate_grad = jnp.dot(pre_grad, w_up.T, preferred_element_type=jnp.float32).astype(
        jnp.bfloat16
    )
    contrib = jnp.where(
        trip_live[:, None],
        jnp.take(aggregate_grad, local_dest, axis=0).astype(jnp.float32)
        * basis.astype(jnp.float32),
        jnp.float32(0.0),
    )
    partial_grad = jax.ops.segment_sum(
        contrib, source, num_segments=edge_slots * groups
    ).astype(jnp.bfloat16)
    blocks = partial_grad.reshape(groups, edge_slots, db)
    total = jnp.take(blocks, here, axis=0).astype(jnp.float32)
    for k in range(1, groups):
        piece = jnp.take(blocks, (here + k) % groups, axis=0)
        total = total + shifted(piece, "graph", groups, k).astype(jnp.float32)
    source_grad = total.astype(jnp.bfloat16)
    part_down = jnp.dot(rows.T, source_grad, preferred_element_type=jnp.float32)
    result = (edge_out + jnp.dot(source_grad, w_down.T, preferred_element_type=jnp.float32)).astype(
        jnp.bfloat16
    )

    width = da // groups
    atom_blocks = part_atom.reshape(de, groups, width)
    atom_sum = jnp.take(atom_blocks, here, axis=1)
    for k in range(1, groups):
        piece = jnp.take(atom_blocks, (here + k) % groups, axis=1)
        atom_sum = atom_sum + shifted(piece, "graph", groups, k)
    up_sum = butterfly(part_up.T, "graph", groups)
    early = butterfly(jnp.concatenate([atom_sum, up_sum], axis=1), "dp", dps)
    down_grad = butterfly(part_down, ("dp", "graph"), dps * groups)
    atom_grad = early[:, :width]
    up_grad = early[:, width:].T
    return (result[None], atom_grad, up_grad, down_grad)


def solution(mesh):
    return jax.shard_map(
        local,
        mesh=mesh,
        in_specs=(
            P("dp", "graph", None),
            P("dp", "graph", None),
            P("dp", "graph", None),
            P("dp", "graph"),
            P("dp", "graph"),
            P("dp", "graph"),
            P("dp", "graph"),
            P("dp", "graph"),
            P("dp", "graph"),
            P(),
            P(),
            P(),
        ),
        out_specs=(P("dp", "graph", None), P(None, "graph"), P(), P()),
        check_vma=False,
    )
```

```python
import jax
import jax.numpy as jnp
from jax import lax
from jax.sharding import PartitionSpec as P


def shifted(x, axis, size, k):
    return lax.ppermute(x, axis, [(i, (i + k) % size) for i in range(size)])


def butterfly(x, axis, size):
    idx = lax.axis_index(axis)
    stride = 1
    while stride < size:
        radix = 4 if (size // stride) % 4 == 0 else 2
        if radix == 2:
            x = x + lax.ppermute(x, axis, [(i, i ^ stride) for i in range(size)])
        else:
            digit = (idx // stride) % radix
            got = [x]
            for s in range(1, radix):
                pairs = []
                for i in range(size):
                    d = (i // stride) % radix
                    pairs.append((i, i + ((d + s) % radix - d) * stride))
                got.append(lax.ppermute(x, axis, pairs))
            stacked = jnp.stack(got)
            member = [jnp.take(stacked, (digit - m) % radix, axis=0) for m in range(radix)]
            x = (member[0] + member[1]) + (member[2] + member[3])
        stride *= radix
    return x


def local(
    embedding,
    triplet_basis,
    atom_cotangent,
    fidelity,
    edge_target,
    triplet_source,
    triplet_target,
    edge_count,
    triplet_count,
    w_down,
    w_up,
    w_atom,
):
    rows = embedding[0]
    basis = triplet_basis[0]
    edge_slots, de = rows.shape
    trip_slots, db = basis.shape
    atom_slots, da = atom_cotangent.shape[1:]
    groups = lax.axis_size("graph")
    dps = lax.axis_size("dp")
    here = lax.axis_index("graph")
    edge_live = jnp.arange(edge_slots, dtype=jnp.int32) < edge_count[0, 0]
    trip_live = jnp.arange(trip_slots, dtype=jnp.int32) < triplet_count[0, 0]
    weight = 1.0 + 3.0 * fidelity[0].astype(jnp.float32)
    scaled = (weight[:, None] * atom_cotangent[0].astype(jnp.float32)).astype(jnp.bfloat16)
    projected = jnp.dot(rows, w_down, preferred_element_type=jnp.float32).astype(jnp.bfloat16)

    table_pieces = [projected] + [shifted(projected, "graph", groups, k) for k in range(1, groups)]
    atoms_all = lax.all_gather(scaled, "graph", axis=0, tiled=True)
    table = jnp.concatenate(table_pieces, axis=0)

    source = triplet_source[0]
    src_row = ((here - source // edge_slots) % groups) * edge_slots + source % edge_slots
    feats = jnp.take(table, src_row, axis=0)
    target = edge_target[0]

    local_dest = triplet_target[0] - here * edge_slots
    product = feats.astype(jnp.float32) * basis.astype(jnp.float32)
    hi = product.astype(jnp.bfloat16)
    lo = (product - hi.astype(jnp.float32)).astype(jnp.bfloat16)
    pick = (local_dest[None, :] == jnp.arange(edge_slots, dtype=jnp.int32)[:, None]) & trip_live[None, :]
    summed = jnp.dot(
        pick.astype(jnp.bfloat16),
        jnp.concatenate([hi, lo], axis=1),
        preferred_element_type=jnp.float32,
    )
    aggregate = (summed[:, :db] + summed[:, db:]).astype(jnp.bfloat16)

    pre = jnp.dot(aggregate, w_up, preferred_element_type=jnp.float32)
    sig = jax.nn.sigmoid(pre)
    updated = (rows.astype(jnp.float32) + pre * sig).astype(jnp.bfloat16)
    edge_in = jnp.where(
        edge_live[:, None], jnp.take(atoms_all, target, axis=0), jnp.zeros((), jnp.bfloat16)
    )
    edge_out = jnp.dot(edge_in, w_atom.T, preferred_element_type=jnp.float32)
    part_atom = jnp.dot(updated.T, edge_in, preferred_element_type=jnp.float32)
    pre_grad = (edge_out * sig * (1.0 + pre * (1.0 - sig))).astype(jnp.bfloat16)
    part_up = jnp.dot(aggregate.T, pre_grad, preferred_element_type=jnp.float32)
    aggregate_grad = jnp.dot(pre_grad, w_up.T, preferred_element_type=jnp.float32).astype(
        jnp.bfloat16
    )
    contrib = jnp.where(
        trip_live[:, None],
        jnp.take(aggregate_grad, local_dest, axis=0).astype(jnp.float32)
        * basis.astype(jnp.float32),
        jnp.float32(0.0),
    )
    partial_grad = jax.ops.segment_sum(
        contrib, source, num_segments=edge_slots * groups
    ).astype(jnp.bfloat16)
    blocks = partial_grad.reshape(groups, edge_slots, db)
    total = jnp.take(blocks, here, axis=0).astype(jnp.float32)
    for k in range(1, groups):
        piece = jnp.take(blocks, (here + k) % groups, axis=0)
        total = total + shifted(piece, "graph", groups, k).astype(jnp.float32)
    source_grad = total.astype(jnp.bfloat16)
    part_down = jnp.dot(rows.T, source_grad, preferred_element_type=jnp.float32)
    result = (edge_out + jnp.dot(source_grad, w_down.T, preferred_element_type=jnp.float32)).astype(
        jnp.bfloat16
    )

    width = da // groups
    atom_blocks = part_atom.reshape(de, groups, width)
    atom_sum = jnp.take(atom_blocks, here, axis=1)
    for k in range(1, groups):
        piece = jnp.take(atom_blocks, (here + k) % groups, axis=1)
        atom_sum = atom_sum + shifted(piece, "graph", groups, k)
    atom_grad = butterfly(atom_sum, "dp", dps)
    late = butterfly(jnp.concatenate([part_up.T, part_down], axis=1), ("dp", "graph"), dps * groups)
    up_grad = late[:, :db].T
    down_grad = late[:, db:]
    return (result[None], atom_grad, up_grad, down_grad)


def solution(mesh):
    return jax.shard_map(
        local,
        mesh=mesh,
        in_specs=(
            P("dp", "graph", None),
            P("dp", "graph", None),
            P("dp", "graph", None),
            P("dp", "graph"),
            P("dp", "graph"),
            P("dp", "graph"),
            P("dp", "graph"),
            P("dp", "graph"),
            P("dp", "graph"),
            P(),
            P(),
            P(),
        ),
        out_specs=(P("dp", "graph", None), P(None, "graph"), P(), P()),
        check_vma=False,
    )
```

```python
import jax
import jax.numpy as jnp
from jax import lax
from jax.sharding import PartitionSpec as P


def shifted(x, axis, size, k):
    return lax.ppermute(x, axis, [(i, (i + k) % size) for i in range(size)])


def butterfly(x, axis, size):
    idx = lax.axis_index(axis)
    stride = 1
    while stride < size:
        radix = 4 if (size // stride) % 4 == 0 else 2
        if radix == 2:
            x = x + lax.ppermute(x, axis, [(i, i ^ stride) for i in range(size)])
        else:
            digit = (idx // stride) % radix
            got = [x]
            for s in range(1, radix):
                pairs = []
                for i in range(size):
                    d = (i // stride) % radix
                    pairs.append((i, i + ((d + s) % radix - d) * stride))
                got.append(lax.ppermute(x, axis, pairs))
            stacked = jnp.stack(got)
            member = [jnp.take(stacked, (digit - m) % radix, axis=0) for m in range(radix)]
            x = (member[0] + member[1]) + (member[2] + member[3])
        stride *= radix
    return x


def local(
    embedding,
    triplet_basis,
    atom_cotangent,
    fidelity,
    edge_target,
    triplet_source,
    triplet_target,
    edge_count,
    triplet_count,
    w_down,
    w_up,
    w_atom,
):
    rows = embedding[0]
    basis = triplet_basis[0]
    edge_slots, de = rows.shape
    trip_slots, db = basis.shape
    atom_slots, da = atom_cotangent.shape[1:]
    groups = lax.axis_size("graph")
    dps = lax.axis_size("dp")
    here = lax.axis_index("graph")
    edge_live = jnp.arange(edge_slots, dtype=jnp.int32) < edge_count[0, 0]
    trip_live = jnp.arange(trip_slots, dtype=jnp.int32) < triplet_count[0, 0]
    weight = 1.0 + 3.0 * fidelity[0].astype(jnp.float32)
    scaled = (weight[:, None] * atom_cotangent[0].astype(jnp.float32)).astype(jnp.bfloat16)
    projected = jnp.dot(rows, w_down, preferred_element_type=jnp.float32).astype(jnp.bfloat16)

    table_pieces = [projected] + [shifted(projected, "graph", groups, k) for k in range(1, groups)]
    atoms_all = lax.all_gather(scaled, "graph", axis=0, tiled=True)
    table = jnp.concatenate(table_pieces, axis=0)

    source = triplet_source[0]
    src_row = ((here - source // edge_slots) % groups) * edge_slots + source % edge_slots
    feats = jnp.take(table, src_row, axis=0)
    target = edge_target[0]

    local_dest = triplet_target[0] - here * edge_slots
    product = feats.astype(jnp.float32) * basis.astype(jnp.float32)
    hi = product.astype(jnp.bfloat16)
    lo = (product - hi.astype(jnp.float32)).astype(jnp.bfloat16)
    pick = (local_dest[None, :] == jnp.arange(edge_slots, dtype=jnp.int32)[:, None]) & trip_live[None, :]
    summed = jnp.dot(
        pick.astype(jnp.bfloat16),
        jnp.concatenate([hi, lo], axis=1),
        preferred_element_type=jnp.float32,
    )
    aggregate = (summed[:, :db] + summed[:, db:]).astype(jnp.bfloat16)

    pre = jnp.dot(aggregate, w_up, preferred_element_type=jnp.float32)
    sig = jax.nn.sigmoid(pre)
    updated = (rows.astype(jnp.float32) + pre * sig).astype(jnp.bfloat16)
    edge_in = jnp.where(
        edge_live[:, None], jnp.take(atoms_all, target, axis=0), jnp.zeros((), jnp.bfloat16)
    )
    edge_out = jnp.dot(edge_in, w_atom.T, preferred_element_type=jnp.float32)
    part_atom = jnp.dot(updated.T, edge_in, preferred_element_type=jnp.float32)
    pre_grad = (edge_out * sig * (1.0 + pre * (1.0 - sig))).astype(jnp.bfloat16)
    part_up = jnp.dot(aggregate.T, pre_grad, preferred_element_type=jnp.float32)
    aggregate_grad = jnp.dot(pre_grad, w_up.T, preferred_element_type=jnp.float32).astype(
        jnp.bfloat16
    )
    contrib = jnp.where(
        trip_live[:, None],
        jnp.take(aggregate_grad, local_dest, axis=0).astype(jnp.float32)
        * basis.astype(jnp.float32),
        jnp.float32(0.0),
    )
    partial_grad = jax.ops.segment_sum(
        contrib, source, num_segments=edge_slots * groups
    ).astype(jnp.bfloat16)
    blocks = partial_grad.reshape(groups, edge_slots, db)
    total = jnp.take(blocks, here, axis=0).astype(jnp.float32)
    for k in range(1, groups):
        piece = jnp.take(blocks, (here + k) % groups, axis=0)
        total = total + shifted(piece, "graph", groups, k).astype(jnp.float32)
    source_grad = total.astype(jnp.bfloat16)
    part_down = jnp.dot(rows.T, source_grad, preferred_element_type=jnp.float32)
    result = (edge_out + jnp.dot(source_grad, w_down.T, preferred_element_type=jnp.float32)).astype(
        jnp.bfloat16
    )

    width = da // groups
    if groups == 8:
        quads = part_atom.reshape(de, 2, 4, width)
        low = here % 4
        high = here // 4
        halves = jnp.take(quads, low, axis=2)
        for s in range(1, 4):
            pairs = [(i, i - i % 4 + (i % 4 + s) % 4) for i in range(groups)]
            halves = halves + lax.ppermute(jnp.take(quads, (low + s) % 4, axis=2), "graph", pairs)
        atom_sum = jnp.take(halves, high, axis=1) + lax.ppermute(
            jnp.take(halves, 1 - high, axis=1), "graph", [(i, i ^ 4) for i in range(groups)]
        )
    else:
        atom_blocks = part_atom.reshape(de, groups, width)
        atom_sum = jnp.take(atom_blocks, here, axis=1)
        for k in range(1, groups):
            piece = jnp.take(atom_blocks, (here + k) % groups, axis=1)
            atom_sum = atom_sum + shifted(piece, "graph", groups, k)
    up_sum = butterfly(part_up.T, "graph", groups)
    early = butterfly(jnp.concatenate([atom_sum, up_sum], axis=1), "dp", dps)
    down_grad = butterfly(part_down, ("dp", "graph"), dps * groups)
    atom_grad = early[:, :width]
    up_grad = early[:, width:].T
    return (result[None], atom_grad, up_grad, down_grad)


def solution(mesh):
    return jax.shard_map(
        local,
        mesh=mesh,
        in_specs=(
            P("dp", "graph", None),
            P("dp", "graph", None),
            P("dp", "graph", None),
            P("dp", "graph"),
            P("dp", "graph"),
            P("dp", "graph"),
            P("dp", "graph"),
            P("dp", "graph"),
            P("dp", "graph"),
            P(),
            P(),
            P(),
        ),
        out_specs=(P("dp", "graph", None), P(None, "graph"), P(), P()),
        check_vma=False,
    )
```

```python
import jax
import jax.numpy as jnp
from jax import lax
from jax.sharding import PartitionSpec as P


def shifted(x, axis, size, k):
    return lax.ppermute(x, axis, [(i, (i + k) % size) for i in range(size)])


def butterfly(x, axis, size, widest=4):
    idx = lax.axis_index(axis)
    stride = 1
    while stride < size:
        radix = 4 if widest == 4 and (size // stride) % 4 == 0 else 2
        if radix == 2:
            x = x + lax.ppermute(x, axis, [(i, i ^ stride) for i in range(size)])
        else:
            digit = (idx // stride) % radix
            got = [x]
            for s in range(1, radix):
                pairs = []
                for i in range(size):
                    d = (i // stride) % radix
                    pairs.append((i, i + ((d + s) % radix - d) * stride))
                got.append(lax.ppermute(x, axis, pairs))
            stacked = jnp.stack(got)
            member = [jnp.take(stacked, (digit - m) % radix, axis=0) for m in range(radix)]
            x = (member[0] + member[1]) + (member[2] + member[3])
        stride *= radix
    return x


def local(
    embedding,
    triplet_basis,
    atom_cotangent,
    fidelity,
    edge_target,
    triplet_source,
    triplet_target,
    edge_count,
    triplet_count,
    w_down,
    w_up,
    w_atom,
):
    rows = embedding[0]
    basis = triplet_basis[0]
    edge_slots, de = rows.shape
    trip_slots, db = basis.shape
    atom_slots, da = atom_cotangent.shape[1:]
    groups = lax.axis_size("graph")
    dps = lax.axis_size("dp")
    here = lax.axis_index("graph")
    edge_live = jnp.arange(edge_slots, dtype=jnp.int32) < edge_count[0, 0]
    trip_live = jnp.arange(trip_slots, dtype=jnp.int32) < triplet_count[0, 0]
    weight = 1.0 + 3.0 * fidelity[0].astype(jnp.float32)
    scaled = (weight[:, None] * atom_cotangent[0].astype(jnp.float32)).astype(jnp.bfloat16)
    projected = jnp.dot(rows, w_down, preferred_element_type=jnp.float32).astype(jnp.bfloat16)

    table_pieces = [projected] + [shifted(projected, "graph", groups, k) for k in range(1, groups)]
    atoms_all = lax.all_gather(scaled, "graph", axis=0, tiled=True)
    table = jnp.concatenate(table_pieces, axis=0)

    source = triplet_source[0]
    src_row = ((here - source // edge_slots) % groups) * edge_slots + source % edge_slots
    feats = jnp.take(table, src_row, axis=0)
    target = edge_target[0]

    local_dest = triplet_target[0] - here * edge_slots
    product = feats.astype(jnp.float32) * basis.astype(jnp.float32)
    hi = product.astype(jnp.bfloat16)
    lo = (product - hi.astype(jnp.float32)).astype(jnp.bfloat16)
    pick = (local_dest[None, :] == jnp.arange(edge_slots, dtype=jnp.int32)[:, None]) & trip_live[None, :]
    summed = jnp.dot(
        pick.astype(jnp.bfloat16),
        jnp.concatenate([hi, lo], axis=1),
        preferred_element_type=jnp.float32,
    )
    aggregate = (summed[:, :db] + summed[:, db:]).astype(jnp.bfloat16)

    pre = jnp.dot(aggregate, w_up, preferred_element_type=jnp.float32)
    sig = jax.nn.sigmoid(pre)
    updated = (rows.astype(jnp.float32) + pre * sig).astype(jnp.bfloat16)
    edge_in = jnp.where(
        edge_live[:, None], jnp.take(atoms_all, target, axis=0), jnp.zeros((), jnp.bfloat16)
    )
    edge_out = jnp.dot(edge_in, w_atom.T, preferred_element_type=jnp.float32)
    part_atom = jnp.dot(updated.T, edge_in, preferred_element_type=jnp.float32)
    pre_grad = (edge_out * sig * (1.0 + pre * (1.0 - sig))).astype(jnp.bfloat16)
    part_up = jnp.dot(aggregate.T, pre_grad, preferred_element_type=jnp.float32)
    aggregate_grad = jnp.dot(pre_grad, w_up.T, preferred_element_type=jnp.float32).astype(
        jnp.bfloat16
    )
    contrib = jnp.where(
        trip_live[:, None],
        jnp.take(aggregate_grad, local_dest, axis=0).astype(jnp.float32)
        * basis.astype(jnp.float32),
        jnp.float32(0.0),
    )
    partial_grad = jax.ops.segment_sum(
        contrib, source, num_segments=edge_slots * groups
    ).astype(jnp.bfloat16)
    blocks = partial_grad.reshape(groups, edge_slots, db)
    total = jnp.take(blocks, here, axis=0).astype(jnp.float32)
    for k in range(1, groups):
        piece = jnp.take(blocks, (here + k) % groups, axis=0)
        total = total + shifted(piece, "graph", groups, k).astype(jnp.float32)
    source_grad = total.astype(jnp.bfloat16)
    part_down = jnp.dot(rows.T, source_grad, preferred_element_type=jnp.float32)
    result = (edge_out + jnp.dot(source_grad, w_down.T, preferred_element_type=jnp.float32)).astype(
        jnp.bfloat16
    )

    width = da // groups
    atom_blocks = part_atom.reshape(de, groups, width)
    atom_sum = jnp.take(atom_blocks, here, axis=1)
    for k in range(1, groups):
        piece = jnp.take(atom_blocks, (here + k) % groups, axis=1)
        atom_sum = atom_sum + shifted(piece, "graph", groups, k)
    up_sum = butterfly(part_up.T, "graph", groups)
    early = butterfly(jnp.concatenate([atom_sum, up_sum], axis=1), "dp", dps, widest=2)
    down_grad = butterfly(part_down, ("dp", "graph"), dps * groups)
    atom_grad = early[:, :width]
    up_grad = early[:, width:].T
    return (result[None], atom_grad, up_grad, down_grad)


def solution(mesh):
    return jax.shard_map(
        local,
        mesh=mesh,
        in_specs=(
            P("dp", "graph", None),
            P("dp", "graph", None),
            P("dp", "graph", None),
            P("dp", "graph"),
            P("dp", "graph"),
            P("dp", "graph"),
            P("dp", "graph"),
            P("dp", "graph"),
            P("dp", "graph"),
            P(),
            P(),
            P(),
        ),
        out_specs=(P("dp", "graph", None), P(None, "graph"), P(), P()),
        check_vma=False,
    )
```
